1024 devices in a mesh: gx: 64 (over z, core), gy: 16 (over y, x).
Axes of the slice: x: 4, y: 4, z: 32, core: 2. Of those that a mesh axis runs over, the one named last changes fastest.
Arguments:
- source: float32 [512, 256, 128], P('gx', 'gy'), may hold values from -6 to 6, as said below
- coupling_x: float32 [512, 256, 128], P('gx', 'gy'), may hold values from 128 to 512
- coupling_y: float32 [512, 256, 128], P('gx', 'gy'), may hold values from 128 to 512
- reaction: float32 [512, 256, 128], P('gx', 'gy'), may hold values from 0.03 to 0.12
Outputs:
- advanced: float32 [512, 256, 128], P('gx', 'gy')
The draws below stay inside these ranges and needn't reach their ends.
Inputs may be any that keep to these rules, and one draw needn't show every extreme that they name: source terms of the sub-step.
All inputs are finite; a program needn't handle non-finite values.
Results may differ from the reference program's by a relative error of at most 0.002.
Values sent between devices are 32-bit elements; how exact they have to be, the bound alone decides.
No kernel may reach another device: no remote copies, remote signals or barrier semaphores. Data moves between devices by JAX's collectives and lax.ppermute only.
A program may use at most 64 MiB of HBM per device.

```python
import math
import jax
import jax.numpy as jnp
from jax import lax

NZ = 128
NX = 512
NY = 256


def draw_source(key, part):
    shape = (NX, NY, NZ)
    values = jax.random.truncated_normal(key, -6.0, 6.0, shape, jnp.float32)
    return values


def levels(stream_key, extent, split, low, top_value):
    gain, own = 1.0, jax.random.fold_in(stream_key, 6)
    for dim, blocks in split:
        steps = jnp.exp(jax.random.uniform(jax.random.fold_in(own, dim), (blocks,), jnp.float32, low / len(split), top_value / len(split)))
        gain = gain * jnp.repeat(steps, extent[dim] // blocks).reshape([-1 if axis == dim else 1 for axis in range(len(extent))])
    return gain


def setup_inputs(seed: int = 0) -> dict:
    key_list = jax.random.split(jax.random.key(seed), 5)
    source = draw_source(jax.random.fold_in(key_list[4], 71), 0)
    coupling_x = jnp.clip(jnp.exp(math.log(512.0) - 1.3862944 * jax.random.uniform(key_list[1], (NX, NY, NZ), jnp.float32) ** levels(key_list[1], (NX, NY, NZ), ((0, 64), (1, 16)), -0.2, 0.2)), 128.0, 512.0)
    coupling_y = jnp.clip(jnp.exp(math.log(512.0) - 1.3862944 * jax.random.uniform(key_list[2], (NX, NY, NZ), jnp.float32) ** levels(key_list[2], (NX, NY, NZ), ((0, 64), (1, 16)), -0.2, 0.2)), 128.0, 512.0)
    reaction = jnp.clip(jnp.exp(math.log(0.12) - 1.3862944 * jax.random.uniform(key_list[3], (NX, NY, NZ), jnp.float32) ** levels(key_list[3], (NX, NY, NZ), ((0, 64), (1, 16)), -0.2, 0.2)), 0.03, 0.12)
    return {"source": source, "coupling_x": coupling_x, "coupling_y": coupling_y, "reaction": reaction}


def sweep(source, neighbor_coupling, reaction):
    zero_row = jnp.zeros_like(source[0])

    def forward_step(carry, cells):
        ratio_prev, shifted_prev = carry
        value, link, decay = cells
        denom = decay + 2.0 * link + link * ratio_prev
        ratio_now = -link / denom
        shifted_now = (value + link * shifted_prev) / denom
        return (ratio_now, shifted_now), (ratio_now, shifted_now)

    final_carry, outputs = lax.scan(forward_step, (zero_row, zero_row), (source, neighbor_coupling, reaction))

    def backward_step(later_value, cells):
        ratio_now, shifted_now = cells
        current = shifted_now - ratio_now * later_value
        return current, current

    last_carry, solved = lax.scan(backward_step, zero_row, outputs, reverse=True)
    return solved


def reference(source, coupling_x, coupling_y, reaction):
    halfway = sweep(source, coupling_x, reaction)
    turned = sweep(jnp.moveaxis(halfway, 1, 0), jnp.moveaxis(coupling_y, 1, 0), jnp.moveaxis(reaction, 1, 0))
    return jnp.moveaxis(turned, 0, 1)
```

```python
import jax
import jax.numpy as jnp
from jax import lax
from jax.experimental import pallas as pl
from jax.sharding import PartitionSpec as P


def local_kernel(f_ref, k_ref, r_ref, a_ref, b_ref, c_ref):
    n = f_ref.shape[0]
    zero = jnp.zeros(f_ref.shape[1:], f_ref.dtype)
    ratio, shifted, shifted_b = zero, zero, zero
    for i in range(n):
        link = k_ref[i]
        denom = r_ref[i] + 2.0 * link + link * ratio
        ratio = -link / denom
        shifted = (f_ref[i] + link * shifted) / denom
        shifted_b = (link if i == 0 else link * shifted_b) / denom
        a_ref[i] = shifted
        b_ref[i] = shifted_b
        c_ref[i] = ratio
    later_a = a_ref[n - 1]
    later_b = b_ref[n - 1]
    later_c = k_ref[n - 1] / denom
    c_ref[n - 1] = later_c
    for i in range(n - 2, -1, -1):
        ratio = c_ref[i]
        later_a = a_ref[i] - ratio * later_a
        later_b = b_ref[i] - ratio * later_b
        later_c = -ratio * later_c
        a_ref[i] = later_a
        b_ref[i] = later_b
        c_ref[i] = later_c


def local_solve(f, k, r):
    shape = jax.ShapeDtypeStruct(f.shape, f.dtype)
    return pl.pallas_call(local_kernel, out_shape=(shape, shape, shape))(f, k, r)


def reduced_kernel(coef_ref, out_ref):
    count = coef_ref.shape[0]
    gains = []
    p_prev = None
    q_prev = None
    for d in range(count):
        row = coef_ref[d]
        a0, b0, c0 = row[0:1], row[1:2], row[2:3]
        a1, b1, c1 = row[3:4], row[4:5], row[5:6]
        if d == 0:
            g, h = a0, c0
            p, q = a1, c1
        else:
            denom = 1.0 - b0 * q_prev
            g = (a0 + b0 * p_prev) / denom
            h = c0 / denom
            p = a1 + b1 * p_prev + b1 * q_prev * g
            q = c1 + b1 * q_prev * h
        gains.append((g, h, p, q))
        p_prev, q_prev = p, q
    later = jnp.zeros_like(gains[0][0])
    for d in range(count - 1, -1, -1):
        g, h, _, _ = gains[d]
        first = g + h * later
        if d > 0:
            _, _, p, q = gains[d - 1]
            before = p + q * first
        else:
            before = jnp.zeros_like(first)
        out_ref[d, 0:1, :] = before
        out_ref[d, 1:2, :] = later
        later = first


def reduced_solve(coef):
    count, _, m = coef.shape
    return pl.pallas_call(
        reduced_kernel, out_shape=jax.ShapeDtypeStruct((count, 2, m), coef.dtype)
    )(coef)


def solve_along_0(f, k, r, axis):
    count = lax.axis_size(axis)
    n, rows, lanes = f.shape
    a, b, c = local_solve(f, k, r)
    lines = rows * lanes
    m = lines // count
    coef = jnp.stack([a[0], b[0], c[0], a[n - 1], b[n - 1], c[n - 1]]).reshape(6, count, m)
    coef = jnp.transpose(coef, (1, 0, 2))
    gathered = lax.all_to_all(coef, axis, 0, 0, tiled=True)
    ends = reduced_solve(gathered)
    ends = lax.all_to_all(ends, axis, 0, 0, tiled=True)
    ends = jnp.transpose(ends, (1, 0, 2)).reshape(2, rows, lanes)
    return a + b * ends[0][None] + c * ends[1][None]


def per_device(source, coupling_x, coupling_y, reaction):
    halfway = solve_along_0(source, coupling_x, reaction, "gx")
    turned = solve_along_0(
        jnp.swapaxes(halfway, 0, 1),
        jnp.swapaxes(coupling_y, 0, 1),
        jnp.swapaxes(reaction, 0, 1),
        "gy",
    )
    return jnp.swapaxes(turned, 0, 1)


def solution(mesh):
    placed = (P("gx", "gy", None), P("gx", "gy", None), P("gx", "gy", None), P("gx", "gy", None))
    return jax.shard_map(
        per_device, mesh=mesh, in_specs=placed, out_specs=P("gx", "gy", None), check_vma=False
    )
```

```python
from functools import partial

import jax
import jax.numpy as jnp
from jax import lax
from jax.experimental import pallas as pl
from jax.sharding import PartitionSpec as P


def local_kernel(f_ref, k_ref, r_ref, a_ref, b_ref, c_ref, e_ref):
    n = f_ref.shape[0]
    zero = jnp.zeros(f_ref.shape[1:], f_ref.dtype)
    ratio, shifted, shifted_b = zero, zero, zero
    for i in range(n):
        link = k_ref[i]
        denom = r_ref[i] + 2.0 * link + link * ratio
        ratio = -link / denom
        shifted = (f_ref[i] + link * shifted) / denom
        shifted_b = (link if i == 0 else link * shifted_b) / denom
        a_ref[i] = shifted
        b_ref[i] = shifted_b
        c_ref[i] = ratio
    later_a = a_ref[n - 1]
    later_b = b_ref[n - 1]
    later_c = k_ref[n - 1] / denom
    c_ref[n - 1] = later_c
    for i in range(n - 2, -1, -1):
        ratio = c_ref[i]
        later_a = a_ref[i] - ratio * later_a
        later_b = b_ref[i] - ratio * later_b
        later_c = -ratio * later_c
        a_ref[i] = later_a
        b_ref[i] = later_b
        c_ref[i] = later_c
    for j, (ref, at) in enumerate(((a_ref, 0), (b_ref, 0), (c_ref, 0), (a_ref, n - 1), (b_ref, n - 1), (c_ref, n - 1))):
        e_ref[j] = ref[at]


def local_solve(f, k, r):
    shape = jax.ShapeDtypeStruct(f.shape, f.dtype)
    ends = jax.ShapeDtypeStruct((6,) + f.shape[1:], f.dtype)
    return pl.pallas_call(local_kernel, out_shape=(shape, shape, shape, ends))(f, k, r)


def compose(earlier, later):
    xa0, xb0, xc0, xa1, xb1, xc1 = earlier
    ya0, yb0, yc0, ya1, yb1, yc1 = later
    denom = 1.0 - xc1 * yb0
    join_a = (xa1 + xc1 * ya0) / denom
    join_b = xb1 / denom
    join_c = xc1 * yc0 / denom
    next_a = ya0 + yb0 * join_a
    next_b = yb0 * join_b
    next_c = yc0 + yb0 * join_c
    return (
        xa0 + xc0 * next_a,
        xb0 + xc0 * next_b,
        xc0 * next_c,
        ya1 + yb1 * join_a,
        yb1 * join_b,
        yc1 + yb1 * join_c,
    )


def round_kernel(final, left_ref, right_ref, ip_ref, ep_ref, is_ref, es_ref, *rest):
    rows = lambda ref: tuple(ref[i] for i in range(6))
    from_left, from_right = rows(left_ref), rows(right_ref)
    incl_pre = compose(from_left, rows(ip_ref))
    excl_pre = compose(from_left, rows(ep_ref))
    incl_suf = compose(rows(is_ref), from_right)
    excl_suf = compose(rows(es_ref), from_right)
    if not final:
        for out_ref, value in zip(rest, (incl_pre, excl_pre, incl_suf, excl_suf)):
            for i in range(6):
                out_ref[i] = value[i]
        return
    a_ref, b_ref, c_ref, out_ref = rest
    q = excl_pre[5]
    before = (excl_pre[3] + q * incl_suf[0]) / (1.0 - q * incl_suf[1])
    v = excl_suf[1]
    after = (excl_suf[0] + v * incl_pre[3]) / (1.0 - v * incl_pre[5])
    for i in range(a_ref.shape[0]):
        out_ref[i] = a_ref[i] + b_ref[i] * before + c_ref[i] * after


def solve_along_0(f, k, r, axis):
    count = lax.axis_size(axis)
    a, b, c, block = local_solve(f, k, r)
    if count == 1:
        return a
    identity = jnp.zeros_like(block).at[2].set(1.0).at[4].set(1.0)
    incl_pre, excl_pre, incl_suf, excl_suf = block, identity, block, identity
    state = jax.ShapeDtypeStruct(block.shape, block.dtype)
    shift = 1
    while shift < count:
        rightward = [(i, i + shift) for i in range(count - shift)]
        leftward = [(i + shift, i) for i in range(count - shift)]
        from_left = lax.ppermute(incl_pre, axis, rightward)
        from_right = lax.ppermute(incl_suf, axis, leftward)
        final = shift * 2 >= count
        operands = (from_left, from_right, incl_pre, excl_pre, incl_suf, excl_suf)
        if final:
            return pl.pallas_call(
                partial(round_kernel, True), out_shape=jax.ShapeDtypeStruct(a.shape, a.dtype)
            )(*operands, a, b, c)
        incl_pre, excl_pre, incl_suf, excl_suf = pl.pallas_call(
            partial(round_kernel, False), out_shape=(state, state, state, state)
        )(*operands)
        shift *= 2


def per_device(source, coupling_x, coupling_y, reaction):
    halfway = solve_along_0(source, coupling_x, reaction, "gx")
    turned = solve_along_0(
        jnp.swapaxes(halfway, 0, 1),
        jnp.swapaxes(coupling_y, 0, 1),
        jnp.swapaxes(reaction, 0, 1),
        "gy",
    )
    return jnp.swapaxes(turned, 0, 1)


def solution(mesh):
    placed = (P("gx", "gy", None), P("gx", "gy", None), P("gx", "gy", None), P("gx", "gy", None))
    return jax.shard_map(
        per_device, mesh=mesh, in_specs=placed, out_specs=P("gx", "gy", None), check_vma=False
    )
```

```python
import jax
import jax.numpy as jnp
from jax import lax
from jax.experimental import pallas as pl
from jax.sharding import Mesh, PartitionSpec as P


def local_kernel(f_ref, k_ref, r_ref, a_ref, b_ref, c_ref, e_ref):
    n = f_ref.shape[0]
    zero = jnp.zeros(f_ref.shape[1:], f_ref.dtype)
    ratio, shifted, shifted_b = zero, zero, zero
    for i in range(n):
        link = k_ref[i]
        denom = r_ref[i] + 2.0 * link + link * ratio
        ratio = -link / denom
        shifted = (f_ref[i] + link * shifted) / denom
        shifted_b = (link if i == 0 else link * shifted_b) / denom
        a_ref[i] = shifted
        b_ref[i] = shifted_b
        c_ref[i] = ratio
    later_a = a_ref[n - 1]
    later_b = b_ref[n - 1]
    later_c = k_ref[n - 1] / denom
    c_ref[n - 1] = later_c
    for i in range(n - 2, -1, -1):
        ratio = c_ref[i]
        later_a = a_ref[i] - ratio * later_a
        later_b = b_ref[i] - ratio * later_b
        later_c = -ratio * later_c
        a_ref[i] = later_a
        b_ref[i] = later_b
        c_ref[i] = later_c
    for j, (ref, at) in enumerate(((a_ref, 0), (b_ref, 0), (c_ref, 0), (a_ref, n - 1), (b_ref, n - 1), (c_ref, n - 1))):
        e_ref[j] = ref[at]


def local_solve(f, k, r):
    shape = jax.ShapeDtypeStruct(f.shape, f.dtype)
    ends = jax.ShapeDtypeStruct((6,) + f.shape[1:], f.dtype)
    return pl.pallas_call(local_kernel, out_shape=(shape, shape, shape, ends))(f, k, r)


def reduced_kernel(coef_ref, out_ref):
    count = coef_ref.shape[0]
    gains = []
    p_prev = None
    q_prev = None
    for d in range(count):
        row = coef_ref[d]
        a0, b0, c0 = row[0:1], row[1:2], row[2:3]
        a1, b1, c1 = row[3:4], row[4:5], row[5:6]
        if d == 0:
            g, h = a0, c0
            p, q = a1, c1
        else:
            denom = 1.0 - b0 * q_prev
            g = (a0 + b0 * p_prev) / denom
            h = c0 / denom
            p = a1 + b1 * p_prev + b1 * q_prev * g
            q = c1 + b1 * q_prev * h
        gains.append((g, h, p, q))
        p_prev, q_prev = p, q
    later = jnp.zeros_like(gains[0][0])
    for d in range(count - 1, -1, -1):
        g, h, _, _ = gains[d]
        first = g + h * later
        if d > 0:
            _, _, p, q = gains[d - 1]
            before = p + q * first
        else:
            before = jnp.zeros_like(first)
        out_ref[d, 0:1, :] = before
        out_ref[d, 1:2, :] = later
        later = first


def reduced_solve(coef):
    count, _, m = coef.shape
    return pl.pallas_call(
        reduced_kernel, out_shape=jax.ShapeDtypeStruct((count, 2, m), coef.dtype)
    )(coef)


def solve_along_0(f, k, r, axis):
    count = lax.axis_size(axis)
    n, rows, lanes = f.shape
    a, b, c, coef = local_solve(f, k, r)
    lines = rows * lanes
    m = lines // count
    coef = coef.reshape(6, count, m)
    coef = jnp.transpose(coef, (1, 0, 2))
    gathered = lax.all_to_all(coef, axis, 0, 0, tiled=True)
    ends = reduced_solve(gathered)
    ends = lax.all_to_all(ends, axis, 0, 0, tiled=True)
    ends = jnp.transpose(ends, (1, 0, 2)).reshape(2, rows, lanes)
    return a + b * ends[0][None] + c * ends[1][None]


GROUP = 8


def per_device(source, coupling_x, coupling_y, reaction):
    fields = jnp.stack([source, coupling_x, coupling_y, reaction])
    fields = lax.all_to_all(fields, "gxi", 3, 1, tiled=True)
    source, coupling_x, coupling_y, reaction = (fields[i] for i in range(4))
    halfway = solve_along_0(source, coupling_x, reaction, "gxo")
    turned = solve_along_0(
        jnp.swapaxes(halfway, 0, 1),
        jnp.swapaxes(coupling_y, 0, 1),
        jnp.swapaxes(reaction, 0, 1),
        "gy",
    )
    advanced = jnp.swapaxes(turned, 0, 1)
    return lax.all_to_all(advanced, "gxi", 0, 2, tiled=True)


def solution(mesh):
    across, down = mesh.shape["gx"], mesh.shape["gy"]
    inner = GROUP if across % GROUP == 0 else 1
    grouped = Mesh(mesh.devices.reshape(across // inner, inner, down), ("gxo", "gxi", "gy"))
    placed = P(("gxo", "gxi"), "gy", None)
    return jax.shard_map(
        per_device, mesh=grouped, in_specs=(placed,) * 4, out_specs=placed, check_vma=False
    )
```

```python
import jax
import jax.numpy as jnp
from jax import lax
from jax.experimental import pallas as pl
from jax.sharding import Mesh, PartitionSpec as P


def local_kernel(f_ref, k_ref, r_ref, a_ref, b_ref, c_ref, e_ref):
    n = f_ref.shape[0]
    zero = jnp.zeros(f_ref.shape[1:], f_ref.dtype)
    ratio, shifted, shifted_b = zero, zero, zero
    for i in range(n):
        link = k_ref[i]
        denom = r_ref[i] + 2.0 * link + link * ratio
        ratio = -link / denom
        shifted = (f_ref[i] + link * shifted) / denom
        shifted_b = (link if i == 0 else link * shifted_b) / denom
        a_ref[i] = shifted
        b_ref[i] = shifted_b
        c_ref[i] = ratio
    later_a = a_ref[n - 1]
    later_b = b_ref[n - 1]
    later_c = k_ref[n - 1] / denom
    c_ref[n - 1] = later_c
    for i in range(n - 2, -1, -1):
        ratio = c_ref[i]
        later_a = a_ref[i] - ratio * later_a
        later_b = b_ref[i] - ratio * later_b
        later_c = -ratio * later_c
        a_ref[i] = later_a
        b_ref[i] = later_b
        c_ref[i] = later_c
    for j, (ref, at) in enumerate(((a_ref, 0), (b_ref, 0), (c_ref, 0), (a_ref, n - 1), (b_ref, n - 1), (c_ref, n - 1))):
        e_ref[j] = ref[at]


def local_solve(f, k, r):
    shape = jax.ShapeDtypeStruct(f.shape, f.dtype)
    ends = jax.ShapeDtypeStruct((6,) + f.shape[1:], f.dtype)
    return pl.pallas_call(local_kernel, out_shape=(shape, shape, shape, ends))(f, k, r)


def reduced_kernel(coef_ref, out_ref):
    count = coef_ref.shape[0]
    gains = []
    p_prev = None
    q_prev = None
    for d in range(count):
        row = coef_ref[d]
        a0, b0, c0 = row[0:1], row[1:2], row[2:3]
        a1, b1, c1 = row[3:4], row[4:5], row[5:6]
        if d == 0:
            g, h = a0, c0
            p, q = a1, c1
        else:
            denom = 1.0 - b0 * q_prev
            g = (a0 + b0 * p_prev) / denom
            h = c0 / denom
            p = a1 + b1 * p_prev + b1 * q_prev * g
            q = c1 + b1 * q_prev * h
        gains.append((g, h, p, q))
        p_prev, q_prev = p, q
    later = jnp.zeros_like(gains[0][0])
    for d in range(count - 1, -1, -1):
        g, h, _, _ = gains[d]
        first = g + h * later
        if d > 0:
            _, _, p, q = gains[d - 1]
            before = p + q * first
        else:
            before = jnp.zeros_like(first)
        out_ref[d, 0:1, :] = before
        out_ref[d, 1:2, :] = later
        later = first


def reduced_solve(coef):
    count, _, m = coef.shape
    return pl.pallas_call(
        reduced_kernel, out_shape=jax.ShapeDtypeStruct((count, 2, m), coef.dtype)
    )(coef)


def solve_along_0(f, k, r, axis):
    count = lax.axis_size(axis)
    n, rows, lanes = f.shape
    a, b, c, coef = local_solve(f, k, r)
    lines = rows * lanes
    m = lines // count
    coef = coef.reshape(6, count, m)
    coef = jnp.transpose(coef, (1, 0, 2))
    gathered = lax.all_to_all(coef, axis, 0, 0, tiled=True)
    ends = reduced_solve(gathered)
    ends = lax.all_to_all(ends, axis, 0, 0, tiled=True)
    ends = jnp.transpose(ends, (1, 0, 2)).reshape(2, rows, lanes)
    return a + b * ends[0][None] + c * ends[1][None]


GROUP = 8


def gathered_kernel(coef_ref, out_ref):
    count = coef_ref.shape[0]
    gains = []
    p_prev = None
    q_prev = None
    for d in range(count):
        a0, b0, c0, a1, b1, c1 = (coef_ref[d, j] for j in range(6))
        if d == 0:
            g, h = a0, c0
            p, q = a1, c1
        else:
            denom = 1.0 - b0 * q_prev
            g = (a0 + b0 * p_prev) / denom
            h = c0 / denom
            p = a1 + b1 * p_prev + b1 * q_prev * g
            q = c1 + b1 * q_prev * h
        gains.append((g, h, p, q))
        p_prev, q_prev = p, q
    later = jnp.zeros_like(gains[0][0])
    for d in range(count - 1, -1, -1):
        g, h, _, _ = gains[d]
        first = g + h * later
        if d > 0:
            _, _, p, q = gains[d - 1]
            before = p + q * first
        else:
            before = jnp.zeros_like(first)
        out_ref[d, 0] = before
        out_ref[d, 1] = later
        later = first


def solve_gathered(f, k, r, axis):
    a, b, c, coef = local_solve(f, k, r)
    everything = lax.all_gather(coef, axis)
    count = everything.shape[0]
    ends = pl.pallas_call(
        gathered_kernel,
        out_shape=jax.ShapeDtypeStruct((count, 2) + coef.shape[1:], coef.dtype),
    )(everything)
    mine = lax.dynamic_index_in_dim(ends, lax.axis_index(axis), 0, keepdims=False)
    return a + b * mine[0][None] + c * mine[1][None]


def per_device(source, coupling_x, coupling_y, reaction):
    fields = jnp.stack([source, coupling_x, coupling_y, reaction])
    fields = lax.all_to_all(fields, "gxi", 3, 1, tiled=True)
    source, coupling_x, coupling_y, reaction = (fields[i] for i in range(4))
    halfway = solve_gathered(source, coupling_x, reaction, "gxo")
    turned = solve_along_0(
        jnp.swapaxes(halfway, 0, 1),
        jnp.swapaxes(coupling_y, 0, 1),
        jnp.swapaxes(reaction, 0, 1),
        "gy",
    )
    advanced = jnp.swapaxes(turned, 0, 1)
    return lax.all_to_all(advanced, "gxi", 0, 2, tiled=True)


def solution(mesh):
    across, down = mesh.shape["gx"], mesh.shape["gy"]
    inner = GROUP if across % GROUP == 0 else 1
    grouped = Mesh(mesh.devices.reshape(across // inner, inner, down), ("gxo", "gxi", "gy"))
    placed = P(("gxo", "gxi"), "gy", None)
    return jax.shard_map(
        per_device, mesh=grouped, in_specs=(placed,) * 4, out_specs=placed, check_vma=False
    )
```

```python
import jax
import jax.numpy as jnp
from jax import lax
from jax.experimental import pallas as pl
from jax.sharding import PartitionSpec as P


def local_kernel(f_ref, k_ref, r_ref, a_ref, b_ref, c_ref, e_ref):
    n = f_ref.shape[0]
    zero = jnp.zeros(f_ref.shape[1:], f_ref.dtype)
    ratio, shifted, shifted_b = zero, zero, zero
    for i in range(n):
        link = k_ref[i]
        denom = r_ref[i] + 2.0 * link + link * ratio
        ratio = -link / denom
        shifted = (f_ref[i] + link * shifted) / denom
        shifted_b = (link if i == 0 else link * shifted_b) / denom
        a_ref[i] = shifted
        b_ref[i] = shifted_b
        c_ref[i] = ratio
    later_a = a_ref[n - 1]
    later_b = b_ref[n - 1]
    later_c = k_ref[n - 1] / denom
    c_ref[n - 1] = later_c
    for i in range(n - 2, -1, -1):
        ratio = c_ref[i]
        later_a = a_ref[i] - ratio * later_a
        later_b = b_ref[i] - ratio * later_b
        later_c = -ratio * later_c
        a_ref[i] = later_a
        b_ref[i] = later_b
        c_ref[i] = later_c
    for j, (ref, at) in enumerate(((a_ref, 0), (b_ref, 0), (c_ref, 0), (a_ref, n - 1), (b_ref, n - 1), (c_ref, n - 1))):
        e_ref[j] = ref[at]


def local_solve(f, k, r):
    shape = jax.ShapeDtypeStruct(f.shape, f.dtype)
    ends = jax.ShapeDtypeStruct((6,) + f.shape[1:], f.dtype)
    return pl.pallas_call(local_kernel, out_shape=(shape, shape, shape, ends))(f, k, r)


def reduced_kernel(coef_ref, out_ref):
    count = coef_ref.shape[0]
    gains = []
    p_prev = None
    q_prev = None
    for d in range(count):
        row = coef_ref[d]
        a0, b0, c0 = row[0:1], row[1:2], row[2:3]
        a1, b1, c1 = row[3:4], row[4:5], row[5:6]
        if d == 0:
            g, h = a0, c0
            p, q = a1, c1
        else:
            denom = 1.0 - b0 * q_prev
            g = (a0 + b0 * p_prev) / denom
            h = c0 / denom
            p = a1 + b1 * p_prev + b1 * q_prev * g
            q = c1 + b1 * q_prev * h
        gains.append((g, h, p, q))
        p_prev, q_prev = p, q
    later = jnp.zeros_like(gains[0][0])
    for d in range(count - 1, -1, -1):
        g, h, _, _ = gains[d]
        first = g + h * later
        if d > 0:
            _, _, p, q = gains[d - 1]
            before = p + q * first
        else:
            before = jnp.zeros_like(first)
        out_ref[d, 0:1, :] = before
        out_ref[d, 1:2, :] = later
        later = first


def reduced_solve(coef):
    count, _, m = coef.shape
    return pl.pallas_call(
        reduced_kernel, out_shape=jax.ShapeDtypeStruct((count, 2, m), coef.dtype)
    )(coef)


def solve_along_0(f, k, r, axis):
    count = lax.axis_size(axis)
    n, rows, lanes = f.shape
    a, b, c, coef = local_solve(f, k, r)
    lines = rows * lanes
    m = lines // count
    coef = coef.reshape(6, count, m)
    coef = jnp.transpose(coef, (1, 0, 2))
    gathered = lax.all_to_all(coef, axis, 0, 0, tiled=True)
    ends = reduced_solve(gathered)
    ends = lax.all_to_all(ends, axis, 0, 0, tiled=True)
    ends = jnp.transpose(ends, (1, 0, 2)).reshape(2, rows, lanes)
    return a + b * ends[0][None] + c * ends[1][None]


def per_device(source, coupling_x, coupling_y, reaction):
    halfway = solve_along_0(source, coupling_x, reaction, "gx")
    turned = solve_along_0(
        jnp.swapaxes(halfway, 0, 1),
        jnp.swapaxes(coupling_y, 0, 1),
        jnp.swapaxes(reaction, 0, 1),
        "gy",
    )
    return jnp.swapaxes(turned, 0, 1)


def solution(mesh):
    placed = (P("gx", "gy", None), P("gx", "gy", None), P("gx", "gy", None), P("gx", "gy", None))
    return jax.shard_map(
        per_device, mesh=mesh, in_specs=placed, out_specs=P("gx", "gy", None), check_vma=False
    )
```

```python
import jax
import jax.numpy as jnp
from jax import lax
from jax.experimental import pallas as pl
from jax.sharding import PartitionSpec as P


def local_kernel(f_ref, k_ref, r_ref, a_ref, b_ref, c_ref, e_ref):
    n = f_ref.shape[0]
    zero = jnp.zeros(f_ref.shape[1:], f_ref.dtype)
    ratio, shifted, shifted_b = zero, zero, zero
    for i in range(n):
        link = k_ref[i]
        denom = r_ref[i] + 2.0 * link + link * ratio
        ratio = -link / denom
        shifted = (f_ref[i] + link * shifted) / denom
        shifted_b = (link if i == 0 else link * shifted_b) / denom
        a_ref[i] = shifted
        b_ref[i] = shifted_b
        c_ref[i] = ratio
    later_a = a_ref[n - 1]
    later_b = b_ref[n - 1]
    later_c = k_ref[n - 1] / denom
    c_ref[n - 1] = later_c
    for i in range(n - 2, -1, -1):
        ratio = c_ref[i]
        later_a = a_ref[i] - ratio * later_a
        later_b = b_ref[i] - ratio * later_b
        later_c = -ratio * later_c
        a_ref[i] = later_a
        b_ref[i] = later_b
        c_ref[i] = later_c
    for j, (ref, at) in enumerate(((a_ref, 0), (b_ref, 0), (c_ref, 0), (a_ref, n - 1), (b_ref, n - 1), (c_ref, n - 1))):
        e_ref[j] = ref[at]


def local_solve(f, k, r):
    shape = jax.ShapeDtypeStruct(f.shape, f.dtype)
    ends = jax.ShapeDtypeStruct((6,) + f.shape[1:], f.dtype)
    return pl.pallas_call(local_kernel, out_shape=(shape, shape, shape, ends))(f, k, r)


def reduced_kernel(coef_ref, out_ref):
    count = coef_ref.shape[0]
    gains = []
    p_prev = None
    q_prev = None
    m = coef_ref.shape[2] // 6
    for d in range(count):
        row = coef_ref[d]
        a0, b0, c0 = row[:, 0:m], row[:, m:2 * m], row[:, 2 * m:3 * m]
        a1, b1, c1 = row[:, 3 * m:4 * m], row[:, 4 * m:5 * m], row[:, 5 * m:6 * m]
        if d == 0:
            g, h = a0, c0
            p, q = a1, c1
        else:
            denom = 1.0 - b0 * q_prev
            g = (a0 + b0 * p_prev) / denom
            h = c0 / denom
            p = a1 + b1 * p_prev + b1 * q_prev * g
            q = c1 + b1 * q_prev * h
        gains.append((g, h, p, q))
        p_prev, q_prev = p, q
    later = jnp.zeros_like(gains[0][0])
    for d in range(count - 1, -1, -1):
        g, h, _, _ = gains[d]
        first = g + h * later
        if d > 0:
            _, _, p, q = gains[d - 1]
            before = p + q * first
        else:
            before = jnp.zeros_like(first)
        out_ref[d, 0:1, :] = before
        out_ref[d, 1:2, :] = later
        later = first


def reduced_solve(coef):
    count, _, width = coef.shape
    return pl.pallas_call(
        reduced_kernel, out_shape=jax.ShapeDtypeStruct((count, 2, width // 6), coef.dtype)
    )(coef)


def solve_along_0(f, k, r, axis):
    count = lax.axis_size(axis)
    n, rows, lanes = f.shape
    a, b, c, coef = local_solve(f, k, r)
    lines = rows * lanes
    m = lines // count
    coef = coef.reshape(6, count, m)
    coef = jnp.transpose(coef, (1, 0, 2)).reshape(count, 1, 6 * m)
    gathered = lax.all_to_all(coef, axis, 0, 0, tiled=True)
    ends = reduced_solve(gathered)
    ends = lax.all_to_all(ends, axis, 0, 0, tiled=True)
    ends = jnp.transpose(ends, (1, 0, 2)).reshape(2, rows, lanes)
    return a + b * ends[0][None] + c * ends[1][None]


def per_device(source, coupling_x, coupling_y, reaction):
    halfway = solve_along_0(source, coupling_x, reaction, "gx")
    turned = solve_along_0(
        jnp.swapaxes(halfway, 0, 1),
        jnp.swapaxes(coupling_y, 0, 1),
        jnp.swapaxes(reaction, 0, 1),
        "gy",
    )
    return jnp.swapaxes(turned, 0, 1)


def solution(mesh):
    placed = (P("gx", "gy", None), P("gx", "gy", None), P("gx", "gy", None), P("gx", "gy", None))
    return jax.shard_map(
        per_device, mesh=mesh, in_specs=placed, out_specs=P("gx", "gy", None), check_vma=False
    )
```

```python
import jax
import jax.numpy as jnp
from jax import lax
from jax.experimental import pallas as pl
from jax.sharding import PartitionSpec as P


def local_kernel(f_ref, k_ref, r_ref, a_ref, b_ref, c_ref, e_ref):
    n = f_ref.shape[0]
    zero = jnp.zeros(f_ref.shape[1:], f_ref.dtype)
    ratio, shifted, shifted_b = zero, zero, zero
    for i in range(n):
        link = k_ref[i]
        denom = r_ref[i] + 2.0 * link + link * ratio
        ratio = -link / denom
        shifted = (f_ref[i] + link * shifted) / denom
        shifted_b = (link if i == 0 else link * shifted_b) / denom
        a_ref[i] = shifted
        b_ref[i] = shifted_b
        c_ref[i] = ratio
    later_a = a_ref[n - 1]
    later_b = b_ref[n - 1]
    later_c = k_ref[n - 1] / denom
    c_ref[n - 1] = later_c
    for i in range(n - 2, -1, -1):
        ratio = c_ref[i]
        later_a = a_ref[i] - ratio * later_a
        later_b = b_ref[i] - ratio * later_b
        later_c = -ratio * later_c
        a_ref[i] = later_a
        b_ref[i] = later_b
        c_ref[i] = later_c
    for j, (ref, at) in enumerate(((a_ref, 0), (b_ref, 0), (c_ref, 0), (a_ref, n - 1), (b_ref, n - 1), (c_ref, n - 1))):
        e_ref[j] = ref[at]


def local_solve(f, k, r):
    shape = jax.ShapeDtypeStruct(f.shape, f.dtype)
    ends = jax.ShapeDtypeStruct((6,) + f.shape[1:], f.dtype)
    return pl.pallas_call(local_kernel, out_shape=(shape, shape, shape, ends))(f, k, r)


def reduced_kernel(coef_ref, out_ref):
    count = coef_ref.shape[0]
    gains = []
    p_prev = None
    q_prev = None
    m = coef_ref.shape[2] // 6
    flat = coef_ref[:, 0, :]
    columns = [flat[:, j * m:(j + 1) * m] for j in range(6)]
    for d in range(count):
        a0, b0, c0, a1, b1, c1 = (column[d:d + 1] for column in columns)
        if d == 0:
            g, h = a0, c0
            p, q = a1, c1
        else:
            denom = 1.0 - b0 * q_prev
            g = (a0 + b0 * p_prev) / denom
            h = c0 / denom
            p = a1 + b1 * p_prev + b1 * q_prev * g
            q = c1 + b1 * q_prev * h
        gains.append((g, h, p, q))
        p_prev, q_prev = p, q
    later = jnp.zeros_like(gains[0][0])
    for d in range(count - 1, -1, -1):
        g, h, _, _ = gains[d]
        first = g + h * later
        if d > 0:
            _, _, p, q = gains[d - 1]
            before = p + q * first
        else:
            before = jnp.zeros_like(first)
        out_ref[d, 0:1, :] = before
        out_ref[d, 1:2, :] = later
        later = first


def reduced_solve(coef):
    count, _, width = coef.shape
    return pl.pallas_call(
        reduced_kernel, out_shape=jax.ShapeDtypeStruct((count, 2, width // 6), coef.dtype)
    )(coef)


def solve_along_0(f, k, r, axis):
    count = lax.axis_size(axis)
    n, rows, lanes = f.shape
    a, b, c, coef = local_solve(f, k, r)
    lines = rows * lanes
    m = lines // count
    coef = coef.reshape(6, count, m)
    coef = jnp.transpose(coef, (1, 0, 2)).reshape(count, 1, 6 * m)
    gathered = lax.all_to_all(coef, axis, 0, 0, tiled=True)
    ends = reduced_solve(gathered)
    ends = lax.all_to_all(ends, axis, 0, 0, tiled=True)
    ends = jnp.transpose(ends, (1, 0, 2)).reshape(2, rows, lanes)
    return a + b * ends[0][None] + c * ends[1][None]


def per_device(source, coupling_x, coupling_y, reaction):
    halfway = solve_along_0(source, coupling_x, reaction, "gx")
    turned = solve_along_0(
        jnp.swapaxes(halfway, 0, 1),
        jnp.swapaxes(coupling_y, 0, 1),
        jnp.swapaxes(reaction, 0, 1),
        "gy",
    )
    return jnp.swapaxes(turned, 0, 1)


def solution(mesh):
    placed = (P("gx", "gy", None), P("gx", "gy", None), P("gx", "gy", None), P("gx", "gy", None))
    return jax.shard_map(
        per_device, mesh=mesh, in_specs=placed, out_specs=P("gx", "gy", None), check_vma=False
    )
```

```python
import jax
import jax.numpy as jnp
from jax import lax
from jax.experimental import pallas as pl
from jax.sharding import PartitionSpec as P


def local_kernel(f_ref, k_ref, r_ref, a_ref, b_ref, c_ref, e_ref):
    n = f_ref.shape[0]
    zero = jnp.zeros(f_ref.shape[1:], f_ref.dtype)
    ratio, shifted, shifted_b = zero, zero, zero
    for i in range(n):
        link = k_ref[i]
        inverse = 1.0 / (r_ref[i] + 2.0 * link + link * ratio)
        ratio = -link * inverse
        shifted = (f_ref[i] + link * shifted) * inverse
        shifted_b = (link if i == 0 else link * shifted_b) * inverse
        a_ref[i] = shifted
        b_ref[i] = shifted_b
        c_ref[i] = ratio
    later_a = a_ref[n - 1]
    later_b = b_ref[n - 1]
    later_c = k_ref[n - 1] * inverse
    c_ref[n - 1] = later_c
    for i in range(n - 2, -1, -1):
        ratio = c_ref[i]
        later_a = a_ref[i] - ratio * later_a
        later_b = b_ref[i] - ratio * later_b
        later_c = -ratio * later_c
        a_ref[i] = later_a
        b_ref[i] = later_b
        c_ref[i] = later_c
    for j, (ref, at) in enumerate(((a_ref, 0), (b_ref, 0), (c_ref, 0), (a_ref, n - 1), (b_ref, n - 1), (c_ref, n - 1))):
        e_ref[j] = ref[at]


def local_solve(f, k, r):
    shape = jax.ShapeDtypeStruct(f.shape, f.dtype)
    ends = jax.ShapeDtypeStruct((6,) + f.shape[1:], f.dtype)
    return pl.pallas_call(local_kernel, out_shape=(shape, shape, shape, ends))(f, k, r)


def reduced_kernel(coef_ref, out_ref):
    count = coef_ref.shape[0]
    gains = []
    p_prev = None
    q_prev = None
    for d in range(count):
        row = coef_ref[d]
        a0, b0, c0 = row[0:1], row[1:2], row[2:3]
        a1, b1, c1 = row[3:4], row[4:5], row[5:6]
        if d == 0:
            g, h = a0, c0
            p, q = a1, c1
        else:
            inverse = 1.0 / (1.0 - b0 * q_prev)
            g = (a0 + b0 * p_prev) * inverse
            h = c0 * inverse
            p = a1 + b1 * p_prev + b1 * q_prev * g
            q = c1 + b1 * q_prev * h
        gains.append((g, h, p, q))
        p_prev, q_prev = p, q
    later = jnp.zeros_like(gains[0][0])
    for d in range(count - 1, -1, -1):
        g, h, _, _ = gains[d]
        first = g + h * later
        if d > 0:
            _, _, p, q = gains[d - 1]
            before = p + q * first
        else:
            before = jnp.zeros_like(first)
        out_ref[d, 0:1, :] = before
        out_ref[d, 1:2, :] = later
        later = first


def reduced_solve(coef):
    count, _, m = coef.shape
    return pl.pallas_call(
        reduced_kernel, out_shape=jax.ShapeDtypeStruct((count, 2, m), coef.dtype)
    )(coef)


def solve_along_0(f, k, r, axis):
    count = lax.axis_size(axis)
    n, rows, lanes = f.shape
    a, b, c, coef = local_solve(f, k, r)
    lines = rows * lanes
    m = lines // count
    coef = coef.reshape(6, count, m)
    coef = jnp.transpose(coef, (1, 0, 2))
    gathered = lax.all_to_all(coef, axis, 0, 0, tiled=True)
    ends = reduced_solve(gathered)
    ends = lax.all_to_all(ends, axis, 0, 0, tiled=True)
    ends = jnp.transpose(ends, (1, 0, 2)).reshape(2, rows, lanes)
    return a + b * ends[0][None] + c * ends[1][None]


def per_device(source, coupling_x, coupling_y, reaction):
    halfway = solve_along_0(source, coupling_x, reaction, "gx")
    turned = solve_along_0(
        jnp.swapaxes(halfway, 0, 1),
        jnp.swapaxes(coupling_y, 0, 1),
        jnp.swapaxes(reaction, 0, 1),
        "gy",
    )
    return jnp.swapaxes(turned, 0, 1)


def solution(mesh):
    placed = (P("gx", "gy", None), P("gx", "gy", None), P("gx", "gy", None), P("gx", "gy", None))
    return jax.shard_map(
        per_device, mesh=mesh, in_specs=placed, out_specs=P("gx", "gy", None), check_vma=False
    )
```

```python
import jax
import jax.numpy as jnp
from jax import lax
from jax.experimental import pallas as pl
from jax.sharding import PartitionSpec as P


def local_kernel(f_ref, k_ref, r_ref, a_ref, b_ref, c_ref, e_ref):
    n = f_ref.shape[0]
    zero = jnp.zeros(f_ref.shape[1:], f_ref.dtype)
    ratio, shifted, shifted_b = zero, zero, zero
    for i in range(n):
        link = k_ref[i]
        denom = r_ref[i] + 2.0 * link + link * ratio
        ratio = -link / denom
        shifted = (f_ref[i] + link * shifted) / denom
        shifted_b = (link if i == 0 else link * shifted_b) / denom
        a_ref[i] = shifted
        b_ref[i] = shifted_b
        c_ref[i] = ratio
    later_a = a_ref[n - 1]
    later_b = b_ref[n - 1]
    later_c = k_ref[n - 1] / denom
    c_ref[n - 1] = later_c
    for i in range(n - 2, -1, -1):
        ratio = c_ref[i]
        later_a = a_ref[i] - ratio * later_a
        later_b = b_ref[i] - ratio * later_b
        later_c = -ratio * later_c
        a_ref[i] = later_a
        b_ref[i] = later_b
        c_ref[i] = later_c
    for j, (ref, at) in enumerate(((a_ref, 0), (b_ref, 0), (c_ref, 0), (a_ref, n - 1), (b_ref, n - 1), (c_ref, n - 1))):
        e_ref[j] = ref[at]


def local_solve(f, k, r):
    shape = jax.ShapeDtypeStruct(f.shape, f.dtype)
    ends = jax.ShapeDtypeStruct((6,) + f.shape[1:], f.dtype)
    return pl.pallas_call(local_kernel, out_shape=(shape, shape, shape, ends))(f, k, r)


def reduced_kernel(coef_ref, out_ref):
    count = coef_ref.shape[0]
    rows = [coef_ref[d] for d in range(count)]
    parts = [tuple(row[j:j + 1] for j in range(6)) for row in rows]
    zero = jnp.zeros_like(parts[0][0])
    mid = count // 2
    left = []
    p_prev = q_prev = None
    for d in range(mid):
        a0, b0, c0, a1, b1, c1 = parts[d]
        if d == 0:
            g, h, p, q = a0, c0, a1, c1
        else:
            denom = 1.0 - b0 * q_prev
            g = (a0 + b0 * p_prev) / denom
            h = c0 / denom
            p = a1 + b1 * p_prev + b1 * q_prev * g
            q = c1 + b1 * q_prev * h
        left.append((g, h, p, q))
        p_prev, q_prev = p, q
    right = [None] * count
    u_next = v_next = None
    for d in range(count - 1, mid - 1, -1):
        a0, b0, c0, a1, b1, c1 = parts[d]
        if d == count - 1:
            s_d, t_d, u, v = a1, b1, a0, b0
        else:
            denom = 1.0 - c1 * v_next
            s_d = (a1 + c1 * u_next) / denom
            t_d = b1 / denom
            u = a0 + c0 * u_next + c0 * v_next * s_d
            v = b0 + c0 * v_next * t_d
        right[d] = (s_d, t_d, u, v)
        u_next, v_next = u, v
    if mid == 0:
        out_ref[0, 0:1, :] = zero
        out_ref[0, 1:2, :] = zero
        return
    p, q = left[mid - 1][2], left[mid - 1][3]
    u, v = right[mid][2], right[mid][3]
    meet_last = (p + q * u) / (1.0 - q * v)
    meet_first = u + v * meet_last
    later = meet_first
    for d in range(mid - 1, -1, -1):
        g, h, _, _ = left[d]
        first = g + h * later
        if d > 0:
            _, _, p, q = left[d - 1]
            before = p + q * first
        else:
            before = zero
        out_ref[d, 0:1, :] = before
        out_ref[d, 1:2, :] = later
        later = first
    last = meet_last
    for d in range(mid, count):
        s_d, t_d, _, _ = right[d]
        out_ref[d, 0:1, :] = last
        last = s_d + t_d * last
        if d + 1 < count:
            _, _, u, v = right[d + 1]
            after = u + v * last
        else:
            after = zero
        out_ref[d, 1:2, :] = after


def reduced_solve(coef):
    count, _, m = coef.shape
    return pl.pallas_call(
        reduced_kernel, out_shape=jax.ShapeDtypeStruct((count, 2, m), coef.dtype)
    )(coef)


def solve_along_0(f, k, r, axis):
    count = lax.axis_size(axis)
    n, rows, lanes = f.shape
    a, b, c, coef = local_solve(f, k, r)
    lines = rows * lanes
    m = lines // count
    coef = coef.reshape(6, count, m)
    coef = jnp.transpose(coef, (1, 0, 2))
    gathered = lax.all_to_all(coef, axis, 0, 0, tiled=True)
    ends = reduced_solve(gathered)
    ends = lax.all_to_all(ends, axis, 0, 0, tiled=True)
    ends = jnp.transpose(ends, (1, 0, 2)).reshape(2, rows, lanes)
    return a + b * ends[0][None] + c * ends[1][None]


def per_device(source, coupling_x, coupling_y, reaction):
    halfway = solve_along_0(source, coupling_x, reaction, "gx")
    turned = solve_along_0(
        jnp.swapaxes(halfway, 0, 1),
        jnp.swapaxes(coupling_y, 0, 1),
        jnp.swapaxes(reaction, 0, 1),
        "gy",
    )
    return jnp.swapaxes(turned, 0, 1)


def solution(mesh):
    placed = (P("gx", "gy", None), P("gx", "gy", None), P("gx", "gy", None), P("gx", "gy", None))
    return jax.shard_map(
        per_device, mesh=mesh, in_specs=placed, out_specs=P("gx", "gy", None), check_vma=False
    )
```

```python
import jax
import jax.numpy as jnp
from jax import lax
from jax.experimental import pallas as pl
from jax.sharding import PartitionSpec as P


def local_kernel(f_ref, k_ref, r_ref, a_ref, b_ref, c_ref, e_ref):
    n = f_ref.shape[0]
    zero = jnp.zeros(f_ref.shape[1:], f_ref.dtype)
    ratio, shifted, shifted_b = zero, zero, zero
    for i in range(n):
        link = k_ref[i]
        denom = r_ref[i] + 2.0 * link + link * ratio
        ratio = -link / denom
        shifted = (f_ref[i] + link * shifted) / denom
        shifted_b = (link if i == 0 else link * shifted_b) / denom
        a_ref[i] = shifted
        b_ref[i] = shifted_b
        c_ref[i] = ratio
    later_a = a_ref[n - 1]
    later_b = b_ref[n - 1]
    later_c = k_ref[n - 1] / denom
    c_ref[n - 1] = later_c
    for i in range(n - 2, -1, -1):
        ratio = c_ref[i]
        later_a = a_ref[i] - ratio * later_a
        later_b = b_ref[i] - ratio * later_b
        later_c = -ratio * later_c
        a_ref[i] = later_a
        b_ref[i] = later_b
        c_ref[i] = later_c
    ends = ((a_ref, 0), (b_ref, 0), (c_ref, 0), (a_ref, n - 1), (b_ref, n - 1), (c_ref, n - 1))
    if e_ref.shape[0] == 6 and len(e_ref.shape) == 3 and e_ref.shape[1:] == a_ref.shape[1:]:
        for j, (ref, at) in enumerate(ends):
            e_ref[j] = ref[at]
        return
    count, _, m = e_ref.shape
    per_row = a_ref.shape[2] // m
    for c, (ref, at) in enumerate(ends):
        value = ref[at]
        for j in range(count):
            row, lane = j // per_row, (j % per_row) * m
            e_ref[j, c:c + 1, :] = value[row:row + 1, lane:lane + m]


def chunked(f, count):
    m = f.shape[1] * f.shape[2] // count
    return m <= f.shape[2] and f.shape[2] % m == 0 and count != 6


def local_solve(f, k, r, count):
    shape = jax.ShapeDtypeStruct(f.shape, f.dtype)
    if chunked(f, count):
        ends = jax.ShapeDtypeStruct((count, 6, f.shape[1] * f.shape[2] // count), f.dtype)
    else:
        ends = jax.ShapeDtypeStruct((6,) + f.shape[1:], f.dtype)
    return pl.pallas_call(local_kernel, out_shape=(shape, shape, shape, ends))(f, k, r)


def reduced_kernel(coef_ref, out_ref):
    count = coef_ref.shape[0]
    rows = [coef_ref[d] for d in range(count)]
    parts = [tuple(row[j:j + 1] for j in range(6)) for row in rows]
    zero = jnp.zeros_like(parts[0][0])
    mid = count // 2
    left = []
    p_prev = q_prev = None
    for d in range(mid):
        a0, b0, c0, a1, b1, c1 = parts[d]
        if d == 0:
            g, h, p, q = a0, c0, a1, c1
        else:
            denom = 1.0 - b0 * q_prev
            g = (a0 + b0 * p_prev) / denom
            h = c0 / denom
            p = a1 + b1 * p_prev + b1 * q_prev * g
            q = c1 + b1 * q_prev * h
        left.append((g, h, p, q))
        p_prev, q_prev = p, q
    right = [None] * count
    u_next = v_next = None
    for d in range(count - 1, mid - 1, -1):
        a0, b0, c0, a1, b1, c1 = parts[d]
        if d == count - 1:
            s_d, t_d, u, v = a1, b1, a0, b0
        else:
            denom = 1.0 - c1 * v_next
            s_d = (a1 + c1 * u_next) / denom
            t_d = b1 / denom
            u = a0 + c0 * u_next + c0 * v_next * s_d
            v = b0 + c0 * v_next * t_d
        right[d] = (s_d, t_d, u, v)
        u_next, v_next = u, v
    if mid == 0:
        out_ref[0, 0:1, :] = zero
        out_ref[0, 1:2, :] = zero
        return
    p, q = left[mid - 1][2], left[mid - 1][3]
    u, v = right[mid][2], right[mid][3]
    meet_last = (p + q * u) / (1.0 - q * v)
    meet_first = u + v * meet_last
    later = meet_first
    for d in range(mid - 1, -1, -1):
        g, h, _, _ = left[d]
        first = g + h * later
        if d > 0:
            _, _, p, q = left[d - 1]
            before = p + q * first
        else:
            before = zero
        out_ref[d, 0:1, :] = before
        out_ref[d, 1:2, :] = later
        later = first
    last = meet_last
    for d in range(mid, count):
        s_d, t_d, _, _ = right[d]
        out_ref[d, 0:1, :] = last
        last = s_d + t_d * last
        if d + 1 < count:
            _, _, u, v = right[d + 1]
            after = u + v * last
        else:
            after = zero
        out_ref[d, 1:2, :] = after


def reduced_solve(coef):
    count, _, m = coef.shape
    return pl.pallas_call(
        reduced_kernel, out_shape=jax.ShapeDtypeStruct((count, 2, m), coef.dtype)
    )(coef)


def solve_along_0(f, k, r, axis):
    count = lax.axis_size(axis)
    n, rows, lanes = f.shape
    a, b, c, coef = local_solve(f, k, r, count)
    if not chunked(f, count):
        coef = jnp.transpose(coef.reshape(6, count, rows * lanes // count), (1, 0, 2))
    gathered = lax.all_to_all(coef, axis, 0, 0, tiled=True)
    ends = reduced_solve(gathered)
    ends = lax.all_to_all(ends, axis, 0, 0, tiled=True)
    ends = jnp.transpose(ends, (1, 0, 2)).reshape(2, rows, lanes)
    return a + b * ends[0][None] + c * ends[1][None]


def per_device(source, coupling_x, coupling_y, reaction):
    halfway = solve_along_0(source, coupling_x, reaction, "gx")
    turned = solve_along_0(
        jnp.swapaxes(halfway, 0, 1),
        jnp.swapaxes(coupling_y, 0, 1),
        jnp.swapaxes(reaction, 0, 1),
        "gy",
    )
    return jnp.swapaxes(turned, 0, 1)


def solution(mesh):
    placed = (P("gx", "gy", None), P("gx", "gy", None), P("gx", "gy", None), P("gx", "gy", None))
    return jax.shard_map(
        per_device, mesh=mesh, in_specs=placed, out_specs=P("gx", "gy", None), check_vma=False
    )
```

```python
import jax
import jax.numpy as jnp
from jax import lax
from jax.experimental import pallas as pl
from jax.sharding import PartitionSpec as P


def local_kernel(f_ref, k_ref, r_ref, a_ref, b_ref, c_ref, e_ref):
    n = f_ref.shape[0]
    zero = jnp.zeros(f_ref.shape[1:], f_ref.dtype)
    ratio, shifted, shifted_b = zero, zero, zero
    sweep = []
    for i in range(n):
        link = k_ref[i]
        denom = r_ref[i] + 2.0 * link + link * ratio
        ratio = -link / denom
        shifted = (f_ref[i] + link * shifted) / denom
        shifted_b = (link if i == 0 else link * shifted_b) / denom
        sweep.append((ratio, shifted, shifted_b))
    later_a, later_b = shifted, shifted_b
    later_c = k_ref[n - 1] / denom
    solved = [None] * n
    solved[n - 1] = (later_a, later_b, later_c)
    for i in range(n - 2, -1, -1):
        ratio, shifted, shifted_b = sweep[i]
        later_a = shifted - ratio * later_a
        later_b = shifted_b - ratio * later_b
        later_c = -ratio * later_c
        solved[i] = (later_a, later_b, later_c)
    for i in range(n):
        a_ref[i], b_ref[i], c_ref[i] = solved[i]
    for j, value in enumerate(solved[0] + solved[n - 1]):
        e_ref[j] = value


def local_solve(f, k, r):
    shape = jax.ShapeDtypeStruct(f.shape, f.dtype)
    ends = jax.ShapeDtypeStruct((6,) + f.shape[1:], f.dtype)
    return pl.pallas_call(local_kernel, out_shape=(shape, shape, shape, ends))(f, k, r)


def reduced_kernel(coef_ref, out_ref):
    count = coef_ref.shape[0]
    rows = [coef_ref[d] for d in range(count)]
    parts = [tuple(row[j:j + 1] for j in range(6)) for row in rows]
    zero = jnp.zeros_like(parts[0][0])
    mid = count // 2
    left = []
    p_prev = q_prev = None
    for d in range(mid):
        a0, b0, c0, a1, b1, c1 = parts[d]
        if d == 0:
            g, h, p, q = a0, c0, a1, c1
        else:
            denom = 1.0 - b0 * q_prev
            g = (a0 + b0 * p_prev) / denom
            h = c0 / denom
            p = a1 + b1 * p_prev + b1 * q_prev * g
            q = c1 + b1 * q_prev * h
        left.append((g, h, p, q))
        p_prev, q_prev = p, q
    right = [None] * count
    u_next = v_next = None
    for d in range(count - 1, mid - 1, -1):
        a0, b0, c0, a1, b1, c1 = parts[d]
        if d == count - 1:
            s_d, t_d, u, v = a1, b1, a0, b0
        else:
            denom = 1.0 - c1 * v_next
            s_d = (a1 + c1 * u_next) / denom
            t_d = b1 / denom
            u = a0 + c0 * u_next + c0 * v_next * s_d
            v = b0 + c0 * v_next * t_d
        right[d] = (s_d, t_d, u, v)
        u_next, v_next = u, v
    if mid == 0:
        out_ref[0, 0:1, :] = zero
        out_ref[0, 1:2, :] = zero
        return
    p, q = left[mid - 1][2], left[mid - 1][3]
    u, v = right[mid][2], right[mid][3]
    meet_last = (p + q * u) / (1.0 - q * v)
    meet_first = u + v * meet_last
    later = meet_first
    for d in range(mid - 1, -1, -1):
        g, h, _, _ = left[d]
        first = g + h * later
        if d > 0:
            _, _, p, q = left[d - 1]
            before = p + q * first
        else:
            before = zero
        out_ref[d, 0:1, :] = before
        out_ref[d, 1:2, :] = later
        later = first
    last = meet_last
    for d in range(mid, count):
        s_d, t_d, _, _ = right[d]
        out_ref[d, 0:1, :] = last
        last = s_d + t_d * last
        if d + 1 < count:
            _, _, u, v = right[d + 1]
            after = u + v * last
        else:
            after = zero
        out_ref[d, 1:2, :] = after


def reduced_solve(coef):
    count, _, m = coef.shape
    return pl.pallas_call(
        reduced_kernel, out_shape=jax.ShapeDtypeStruct((count, 2, m), coef.dtype)
    )(coef)


def solve_along_0(f, k, r, axis):
    count = lax.axis_size(axis)
    n, rows, lanes = f.shape
    a, b, c, coef = local_solve(f, k, r)
    lines = rows * lanes
    m = lines // count
    coef = coef.reshape(6, count, m)
    coef = jnp.transpose(coef, (1, 0, 2))
    gathered = lax.all_to_all(coef, axis, 0, 0, tiled=True)
    ends = reduced_solve(gathered)
    ends = lax.all_to_all(ends, axis, 0, 0, tiled=True)
    ends = jnp.transpose(ends, (1, 0, 2)).reshape(2, rows, lanes)
    return a + b * ends[0][None] + c * ends[1][None]


def per_device(source, coupling_x, coupling_y, reaction):
    halfway = solve_along_0(source, coupling_x, reaction, "gx")
    turned = solve_along_0(
        jnp.swapaxes(halfway, 0, 1),
        jnp.swapaxes(coupling_y, 0, 1),
        jnp.swapaxes(reaction, 0, 1),
        "gy",
    )
    return jnp.swapaxes(turned, 0, 1)


def solution(mesh):
    placed = (P("gx", "gy", None), P("gx", "gy", None), P("gx", "gy", None), P("gx", "gy", None))
    return jax.shard_map(
        per_device, mesh=mesh, in_specs=placed, out_specs=P("gx", "gy", None), check_vma=False
    )
```
